32 devices in a mesh: state: 2 (over x), member: 16 (over z, y, core).
Axes of the slice: x: 2, y: 2, z: 4, core: 2. Of those that a mesh axis runs over, the one named last changes fastest.
Arguments:
- state: float32 [2048, 1280], P('member', 'state'), may hold values from -6 to 6
- obs_values: float32 [2, 384], replicated, may hold values from -8 to 8
- noise_var: float32 [2, 384], replicated, may hold values from 0.3 to 3
- obs_rows: int32 [2, 384], replicated, may hold values from 0 to 639
- owner: int32 [2, 3], replicated, may hold values from 0 to 1
Outputs:
- analysis: float32 [2048, 1280], P('member', 'state')
The draws below stay inside these ranges and needn't reach their ends.
All inputs are finite; a program needn't handle non-finite values.
Results may differ from the reference program's by a relative error of at most 0.0003.
Values sent between devices are 32-bit elements; how exact they have to be, the bound alone decides.
No kernel may reach another device: no remote copies, remote signals or barrier semaphores. Data moves between devices by JAX's collectives and lax.ppermute only.
A program may use at most 64 MiB of HBM per device.

```python
import math
import jax
import jax.numpy as jnp
from jax import lax

ROWS_DEV = 640
MEMBERS = 2048
OBS = 384
TILE = 128
BLOCKS = 2
OBS_TILES = 3
NSTATE = 1280
N_STATE = 2


def with_ends(values, rng, smallest, top_value):
    longest = values.shape.index(max(values.shape))
    spots = []
    for shift in (0, 1):
        where = [jax.random.randint(jax.random.fold_in(rng, axis), (), 0, length) for axis, length in enumerate(values.shape)]
        where[longest] = (where[longest] + shift) % values.shape[longest]
        spots.append(tuple(where))
    return values.at[spots[0]].set(smallest).at[spots[1]].set(top_value)


def level_of(key, dims, split, least, high):
    def one(dim, parts):
        heights = jax.random.uniform(jax.random.fold_in(jax.random.fold_in(key, 6), dim), (parts,), jnp.float32, least / len(split), high / len(split))
        return jnp.repeat(jnp.exp(heights), dims[dim] // parts).reshape((-1,) + (1,) * (len(dims) - dim - 1))

    gain = one(*split[0])
    for cut in split[1:]:
        gain = gain * one(*cut)
    return gain


def bell_draw(key, dims, spread, limit, pieces=(), kind=jnp.bfloat16):
    result = jax.random.normal(key, dims, jnp.float32) * spread
    if len(pieces) > 0:
        result = level_of(key, dims, pieces, -0.22, 0.18) * result
    return jnp.clip(result, min=-limit, max=limit).astype(kind)


def setup_inputs(seed: int = 0) -> dict:
    splits = jax.random.split(jax.random.key(seed), 6)
    state = bell_draw(splits[0], (MEMBERS, NSTATE), 1.0, 6.0, ((0, 16), (1, 2)), jnp.float32)
    obs_values = bell_draw(splits[1], (BLOCKS, OBS), 1.5, 8.0, (), jnp.float32)
    noise_var = jnp.clip(jnp.exp(jax.random.uniform(splits[2], (BLOCKS, OBS), jnp.float32, math.log(0.3), math.log(3.0))), 0.3, 3.0)
    obs_rows = with_ends(jax.random.randint(splits[3], (BLOCKS, OBS), 0, ROWS_DEV), jax.random.fold_in(splits[3], 1), 0, ROWS_DEV - 1).astype(jnp.int32)
    owner = with_ends(jax.random.randint(splits[4], (BLOCKS, OBS_TILES), 0, N_STATE), jax.random.fold_in(splits[4], 1), 0, N_STATE - 1).astype(jnp.int32)
    return {"state": state, "obs_values": obs_values, "noise_var": noise_var, "obs_rows": obs_rows, "owner": owner}


def full_dot(left, right):
    return jnp.dot(left.astype(jnp.float32), right.astype(jnp.float32), precision=lax.Precision.HIGHEST, preferred_element_type=jnp.float32)

def solve_gram(factor, right):
    half = lax.linalg.triangular_solve(factor, right, left_side=True, lower=True)
    return lax.linalg.triangular_solve(factor, half, left_side=True, lower=True, transpose_a=True)

def analyse(current, observed, target, noise):
    count = current.shape[0]
    row_mean = jnp.sum(current, axis=0) / count
    obs_mean = jnp.sum(observed, axis=0) / count
    row_anom = current - row_mean[None, :]
    obs_anom = observed - obs_mean[None, :]
    cross = full_dot(obs_anom.T, row_anom) / (count - 1.0)
    innov_cov = full_dot(obs_anom.T, obs_anom) / (count - 1.0) + jnp.diag(noise)
    factor = jnp.linalg.cholesky(innov_cov)
    weights = solve_gram(factor, (target - obs_mean)[:, None])
    transformed = solve_gram(factor, obs_anom.T)
    shift = full_dot(weights.T, cross)
    return row_mean[None, :] + shift + row_anom - 0.5 * full_dot(transformed.T, cross)

def reference(state, obs_values, noise_var, obs_rows, owner):
    current = state
    for block in range(BLOCKS):
        owners_each = jnp.repeat(owner[block], TILE).astype(jnp.int32)
        picks = (owners_each * ROWS_DEV + obs_rows[block]).astype(jnp.int32)
        observed = jnp.take(current, picks, axis=1)
        current = analyse(current, observed, obs_values[block], noise_var[block])
    return current
```

```python
import jax
import jax.numpy as jnp
from jax import lax
from jax.sharding import PartitionSpec as P


def full_dot(left, right):
    return jnp.dot(left, right, precision=lax.Precision.HIGHEST, preferred_element_type=jnp.float32)


def tdot(left, right):
    return lax.dot_general(
        left, right, (((0,), (0,)), ((), ())),
        precision=lax.Precision.HIGHEST, preferred_element_type=jnp.float32,
    )


def solve_gram(factor, right):
    half = lax.linalg.triangular_solve(factor, right, left_side=True, lower=True)
    return lax.linalg.triangular_solve(factor, half, left_side=True, lower=True, transpose_a=True)


def exchange(cands, owners_block):
    n_state = lax.axis_size("state")
    obs = cands.shape[1]
    tile = obs // owners_block.shape[0]
    gathered = lax.all_gather(cands, "state", axis=0)
    own_each = jnp.repeat(owners_block, tile)
    pick = own_each[None, :] == jnp.arange(n_state, dtype=own_each.dtype)[:, None]
    return jnp.sum(jnp.where(pick[:, None, :], gathered, 0.0), axis=0)


def analyse(current, observed, target, noise):
    m_loc = current.shape[0]
    n_member = lax.axis_size("member")
    count = m_loc * n_member
    me = lax.axis_index("member")
    n_rows = current.shape[1]
    obs = observed.shape[1]

    row_loc = jnp.mean(current, axis=0)
    obs_loc = jnp.mean(observed, axis=0)
    row_c = current - row_loc[None, :]
    obs_c = observed - obs_loc[None, :]
    gram_loc = tdot(obs_c, obs_c)
    cross_loc = tdot(obs_c, row_c)

    slots = jnp.zeros((n_member, obs + n_rows), jnp.float32)
    slots = lax.dynamic_update_slice(slots, jnp.concatenate([obs_loc, row_loc])[None, :], (me, 0))
    gram_sum, slots = lax.psum((gram_loc, slots), "member")
    cross_loc, gram_sum, slots = lax.optimization_barrier((cross_loc, gram_sum, slots))
    cross_sum = lax.psum(cross_loc, "member")

    means = jnp.mean(slots, axis=0)
    dev = slots - means[None, :]
    obs_mean = means[:obs]
    dev_obs = dev[:, :obs]
    dev_row = dev[:, obs:]

    innov_cov = (gram_sum + m_loc * tdot(dev_obs, dev_obs)) / (count - 1.0) + jnp.diag(noise)
    factor = jnp.linalg.cholesky(innov_cov)
    obs_anom = observed - obs_mean[None, :]
    rhs = (target - obs_mean)[:, None] - 0.5 * obs_anom.T
    gain = solve_gram(factor, rhs)

    cross = (cross_sum + m_loc * tdot(dev_obs, dev_row)) / (count - 1.0)
    return gain, cross


def shards(state, obs_values, noise_var, obs_rows, owner):
    num_blocks = obs_rows.shape[0]
    current = state
    cands = jnp.take(current, obs_rows[0], axis=1)
    for block in range(num_blocks):
        observed = exchange(cands, owner[block])
        gain, cross = analyse(current, observed, obs_values[block], noise_var[block])
        if block + 1 < num_blocks:
            rows = obs_rows[block + 1]
            cands = jnp.take(current, rows, axis=1) + full_dot(gain.T, jnp.take(cross, rows, axis=1))
        current = current + full_dot(gain.T, cross)
    return current


def solution(mesh):
    placed = (P("member", "state"), P(), P(), P(), P())
    return jax.shard_map(
        shards, mesh=mesh, in_specs=placed, out_specs=P("member", "state"), check_vma=False
    )
```

```python
import jax
import jax.numpy as jnp
from jax import lax
from jax.sharding import PartitionSpec as P


def full_dot(left, right):
    return jnp.dot(left, right, precision=lax.Precision.HIGHEST, preferred_element_type=jnp.float32)


def tdot(left, right):
    return lax.dot_general(
        left, right, (((0,), (0,)), ((), ())),
        precision=lax.Precision.HIGHEST, preferred_element_type=jnp.float32,
    )


def _pow2(n):
    return n > 0 and (n & (n - 1)) == 0


def tree_sum(x, axis):
    n = lax.axis_size(axis)
    if n == 1:
        return x
    if not _pow2(n) or x.shape[0] % n != 0:
        return lax.psum(x, axis)
    me = lax.axis_index(axis)
    cur = x
    k = 1
    while k < n:
        perm = [(i, i ^ k) for i in range(n)]
        h = cur.shape[0] // 2
        bit = (me // k) % 2
        keep = lax.dynamic_slice_in_dim(cur, bit * h, h, axis=0)
        send = lax.dynamic_slice_in_dim(cur, (1 - bit) * h, h, axis=0)
        cur = keep + lax.ppermute(send, axis, perm)
        k *= 2
    k = n // 2
    while k >= 1:
        perm = [(i, i ^ k) for i in range(n)]
        bit = (me // k) % 2
        other = lax.ppermute(cur, axis, perm)
        cur = jnp.where(bit == 0, jnp.concatenate([cur, other]), jnp.concatenate([other, cur]))
        k //= 2
    return cur


def tree_sum_exact(x, axis):
    n = lax.axis_size(axis)
    if not _pow2(n):
        return lax.psum(x, axis)
    k = 1
    while k < n:
        perm = [(i, i ^ k) for i in range(n)]
        x = x + lax.ppermute(x, axis, perm)
        k *= 2
    return x


def solve_gram(factor, right):
    half = lax.linalg.triangular_solve(factor, right, left_side=True, lower=True)
    return lax.linalg.triangular_solve(factor, half, left_side=True, lower=True, transpose_a=True)


def exchange(cands, owners_block):
    obs = cands.shape[1]
    tile = obs // owners_block.shape[0]
    own_each = jnp.repeat(owners_block, tile)
    mine = own_each[None, :] == lax.axis_index("state")
    return tree_sum_exact(jnp.where(mine, cands, 0.0), "state")


def analyse(current, observed, target, noise):
    m_loc = current.shape[0]
    n_member = lax.axis_size("member")
    count = m_loc * n_member
    me = lax.axis_index("member")
    n_rows = current.shape[1]
    obs = observed.shape[1]

    row_loc = jnp.mean(current, axis=0)
    obs_loc = jnp.mean(observed, axis=0)
    row_c = current - row_loc[None, :]
    obs_c = observed - obs_loc[None, :]
    gram_loc = tdot(obs_c, obs_c)
    cross_loc = tdot(obs_c, row_c)

    width = -(-(obs + n_rows) // obs) * obs
    slots = jnp.zeros((n_member, width), jnp.float32)
    slots = lax.dynamic_update_slice(slots, jnp.concatenate([obs_loc, row_loc])[None, :], (me, 0))
    packed = jnp.concatenate([gram_loc, slots.reshape(-1, obs)], axis=0)
    packed = tree_sum(packed, "member")
    gram_sum = packed[:obs]
    slots = packed[obs:].reshape(n_member, width)[:, : obs + n_rows]
    cross_loc, gram_sum, slots = lax.optimization_barrier((cross_loc, gram_sum, slots))
    cross_sum = tree_sum(cross_loc, "member")

    means = jnp.mean(slots, axis=0)
    dev = slots - means[None, :]
    obs_mean = means[:obs]
    dev_obs = dev[:, :obs]
    dev_row = dev[:, obs:]

    innov_cov = (gram_sum + m_loc * tdot(dev_obs, dev_obs)) / (count - 1.0) + jnp.diag(noise)
    factor = jnp.linalg.cholesky(innov_cov)
    obs_anom = observed - obs_mean[None, :]
    rhs = (target - obs_mean)[:, None] - 0.5 * obs_anom.T
    gain = solve_gram(factor, rhs)

    cross = (cross_sum + m_loc * tdot(dev_obs, dev_row)) / (count - 1.0)
    return gain, cross


def shards(state, obs_values, noise_var, obs_rows, owner):
    num_blocks = obs_rows.shape[0]
    current = state
    cands = jnp.take(current, obs_rows[0], axis=1)
    for block in range(num_blocks):
        observed = exchange(cands, owner[block])
        gain, cross = analyse(current, observed, obs_values[block], noise_var[block])
        if block + 1 < num_blocks:
            rows = obs_rows[block + 1]
            cands = jnp.take(current, rows, axis=1) + full_dot(gain.T, jnp.take(cross, rows, axis=1))
        current = current + full_dot(gain.T, cross)
    return current


def solution(mesh):
    placed = (P("member", "state"), P(), P(), P(), P())
    return jax.shard_map(
        shards, mesh=mesh, in_specs=placed, out_specs=P("member", "state"), check_vma=False
    )
```

```python
import jax
import jax.numpy as jnp
from jax import lax
from jax.sharding import PartitionSpec as P


def full_dot(left, right):
    return jnp.dot(left, right, precision=lax.Precision.HIGHEST, preferred_element_type=jnp.float32)


def tdot(left, right):
    return lax.dot_general(
        left, right, (((0,), (0,)), ((), ())),
        precision=lax.Precision.HIGHEST, preferred_element_type=jnp.float32,
    )


def _pow2(n):
    return n > 0 and (n & (n - 1)) == 0


def tree_sum(x, axis):
    n = lax.axis_size(axis)
    if n == 1:
        return x
    if not _pow2(n) or x.shape[0] % n != 0:
        return lax.psum(x, axis)
    me = lax.axis_index(axis)
    cur = x
    k = 1
    while k < n:
        perm = [(i, i ^ k) for i in range(n)]
        h = cur.shape[0] // 2
        bit = (me // k) % 2
        keep = lax.dynamic_slice_in_dim(cur, bit * h, h, axis=0)
        send = lax.dynamic_slice_in_dim(cur, (1 - bit) * h, h, axis=0)
        cur = keep + lax.ppermute(send, axis, perm)
        k *= 2
    k = n // 2
    while k >= 1:
        perm = [(i, i ^ k) for i in range(n)]
        bit = (me // k) % 2
        other = lax.ppermute(cur, axis, perm)
        cur = jnp.where(bit == 0, jnp.concatenate([cur, other]), jnp.concatenate([other, cur]))
        k //= 2
    return cur


def tree_sum_exact(x, axis):
    n = lax.axis_size(axis)
    if not _pow2(n):
        return lax.psum(x, axis)
    k = 1
    while k < n:
        perm = [(i, i ^ k) for i in range(n)]
        x = x + lax.ppermute(x, axis, perm)
        k *= 2
    return x


def solve_gram(factor, right):
    half = lax.linalg.triangular_solve(factor, right, left_side=True, lower=True)
    return lax.linalg.triangular_solve(factor, half, left_side=True, lower=True, transpose_a=True)


def block_solve(cov, right, size):
    nb = cov.shape[0] // size
    if nb * size != cov.shape[0]:
        return solve_gram(jnp.linalg.cholesky(cov), right)
    cov = 0.5 * (cov + cov.T)
    eye = jnp.eye(size, dtype=cov.dtype)
    blk = [[cov[i * size:(i + 1) * size, j * size:(j + 1) * size] for j in range(nb)] for i in range(nb)]
    rhs = [right[i * size:(i + 1) * size] for i in range(nb)]
    low = [[None] * nb for _ in range(nb)]
    inv = [None] * nb
    fwd = [None] * nb
    for k in range(nb):
        diag = jnp.linalg.cholesky(blk[k][k], symmetrize_input=False)
        inv[k] = lax.linalg.triangular_solve(diag, eye, left_side=True, lower=True)
        fwd[k] = full_dot(inv[k], rhs[k])
        for i in range(k + 1, nb):
            low[i][k] = full_dot(blk[i][k], inv[k].T)
        for i in range(k + 1, nb):
            for j in range(k + 1, i + 1):
                blk[i][j] = blk[i][j] - full_dot(low[i][k], low[j][k].T)
            rhs[i] = rhs[i] - full_dot(low[i][k], fwd[k])
    out = [None] * nb
    for k in reversed(range(nb)):
        acc = fwd[k]
        for j in range(k + 1, nb):
            acc = acc - tdot(low[j][k], out[j])
        out[k] = tdot(inv[k], acc)
    return jnp.concatenate(out, axis=0)


def exchange(cands, owners_block):
    obs = cands.shape[1]
    tile = obs // owners_block.shape[0]
    own_each = jnp.repeat(owners_block, tile)
    mine = own_each[None, :] == lax.axis_index("state")
    return tree_sum_exact(jnp.where(mine, cands, 0.0), "state")


def analyse(current, observed, target, noise):
    m_loc = current.shape[0]
    n_member = lax.axis_size("member")
    count = m_loc * n_member
    me = lax.axis_index("member")
    n_rows = current.shape[1]
    obs = observed.shape[1]

    row_loc = jnp.mean(current, axis=0)
    obs_loc = jnp.mean(observed, axis=0)
    row_c = current - row_loc[None, :]
    obs_c = observed - obs_loc[None, :]
    gram_loc = tdot(obs_c, obs_c)
    cross_loc = tdot(obs_c, row_c)

    width = -(-(obs + n_rows) // obs) * obs
    slots = jnp.zeros((n_member, width), jnp.float32)
    slots = lax.dynamic_update_slice(slots, jnp.concatenate([obs_loc, row_loc])[None, :], (me, 0))
    packed = jnp.concatenate([gram_loc, slots.reshape(-1, obs)], axis=0)
    packed = tree_sum(packed, "member")
    gram_sum = packed[:obs]
    slots = packed[obs:].reshape(n_member, width)[:, : obs + n_rows]
    cross_loc, gram_sum, slots = lax.optimization_barrier((cross_loc, gram_sum, slots))
    cross_sum = tree_sum(cross_loc, "member")

    means = jnp.mean(slots, axis=0)
    dev = slots - means[None, :]
    obs_mean = means[:obs]
    dev_obs = dev[:, :obs]
    dev_row = dev[:, obs:]

    innov_cov = (gram_sum + m_loc * tdot(dev_obs, dev_obs)) / (count - 1.0) + jnp.diag(noise)
    obs_anom = observed - obs_mean[None, :]
    rhs = (target - obs_mean)[:, None] - 0.5 * obs_anom.T
    gain = block_solve(innov_cov, rhs, 128)

    cross = (cross_sum + m_loc * tdot(dev_obs, dev_row)) / (count - 1.0)
    return gain, cross


def shards(state, obs_values, noise_var, obs_rows, owner):
    num_blocks = obs_rows.shape[0]
    current = state
    cands = jnp.take(current, obs_rows[0], axis=1)
    for block in range(num_blocks):
        observed = exchange(cands, owner[block])
        gain, cross = analyse(current, observed, obs_values[block], noise_var[block])
        if block + 1 < num_blocks:
            rows = obs_rows[block + 1]
            cands = jnp.take(current, rows, axis=1) + full_dot(gain.T, jnp.take(cross, rows, axis=1))
        current = current + full_dot(gain.T, cross)
    return current


def solution(mesh):
    placed = (P("member", "state"), P(), P(), P(), P())
    return jax.shard_map(
        shards, mesh=mesh, in_specs=placed, out_specs=P("member", "state"), check_vma=False
    )
```

```python
import jax
import jax.numpy as jnp
from jax import lax
from jax.sharding import PartitionSpec as P


def full_dot(left, right):
    return jnp.dot(left, right, precision=lax.Precision.HIGHEST, preferred_element_type=jnp.float32)


def tdot(left, right):
    return lax.dot_general(
        left, right, (((0,), (0,)), ((), ())),
        precision=lax.Precision.HIGHEST, preferred_element_type=jnp.float32,
    )


def _pow2(n):
    return n > 0 and (n & (n - 1)) == 0


def tree_sum(x, axis):
    n = lax.axis_size(axis)
    if n == 1:
        return x
    if not _pow2(n) or x.shape[0] % n != 0:
        return lax.psum(x, axis)
    me = lax.axis_index(axis)
    stages = []
    stride = 1
    while stride < n:
        radix = 4 if stride * 4 <= n else 2
        stages.append((stride, radix))
        stride *= radix
    cur = x
    for stride, radix in stages:
        digit = (me // stride) % radix
        h = cur.shape[0] // radix
        total = lax.dynamic_slice_in_dim(cur, digit * h, h, axis=0)
        for o in range(1, radix):
            perm = [(i, i + (((i // stride) % radix) ^ o) * stride - ((i // stride) % radix) * stride) for i in range(n)]
            away = lax.dynamic_slice_in_dim(cur, (digit ^ o) * h, h, axis=0)
            total = total + lax.ppermute(away, axis, perm)
        cur = total
    for stride, radix in reversed(stages):
        digit = (me // stride) % radix
        h = cur.shape[0]
        out = jnp.zeros((h * radix,) + cur.shape[1:], cur.dtype)
        out = lax.dynamic_update_slice_in_dim(out, cur, digit * h, axis=0)
        for o in range(1, radix):
            perm = [(i, i + (((i // stride) % radix) ^ o) * stride - ((i // stride) % radix) * stride) for i in range(n)]
            other = lax.ppermute(cur, axis, perm)
            out = lax.dynamic_update_slice_in_dim(out, other, (digit ^ o) * h, axis=0)
        cur = out
    return cur


def tree_sum_exact(x, axis):
    n = lax.axis_size(axis)
    if not _pow2(n):
        return lax.psum(x, axis)
    k = 1
    while k < n:
        perm = [(i, i ^ k) for i in range(n)]
        x = x + lax.ppermute(x, axis, perm)
        k *= 2
    return x


def block_solve(blk, right, size):
    nb = len(blk)
    eye = jnp.eye(size, dtype=right.dtype)
    rhs = [right[i * size:(i + 1) * size] for i in range(nb)]
    low = [[None] * nb for _ in range(nb)]
    inv = [None] * nb
    fwd = [None] * nb
    for k in range(nb):
        diag = lax.linalg.cholesky(blk[k][k], symmetrize_input=False)
        inv[k] = lax.linalg.triangular_solve(diag, eye, left_side=True, lower=True)
        fwd[k] = full_dot(inv[k], rhs[k])
        for i in range(k + 1, nb):
            low[i][k] = full_dot(blk[i][k], inv[k].T)
        for i in range(k + 1, nb):
            for j in range(k + 1, i + 1):
                blk[i][j] = blk[i][j] - full_dot(low[i][k], low[j][k].T)
            rhs[i] = rhs[i] - full_dot(low[i][k], fwd[k])
    out = [None] * nb
    for k in reversed(range(nb)):
        acc = fwd[k]
        for j in range(k + 1, nb):
            acc = acc - tdot(low[j][k], out[j])
        out[k] = tdot(inv[k], acc)
    return jnp.concatenate(out, axis=0)


def exchange(cands, owners_block):
    obs = cands.shape[1]
    tile = obs // owners_block.shape[0]
    own_each = jnp.repeat(owners_block, tile)
    mine = own_each[None, :] == lax.axis_index("state")
    return tree_sum_exact(jnp.where(mine, cands, 0.0), "state")


def analyse(current, observed, target, noise):
    m_loc = current.shape[0]
    n_member = lax.axis_size("member")
    count = m_loc * n_member
    me = lax.axis_index("member")
    n_rows = current.shape[1]
    obs = observed.shape[1]

    row_loc = jnp.mean(current, axis=0)
    obs_loc = jnp.mean(observed, axis=0)
    row_c = current - row_loc[None, :]
    obs_c = observed - obs_loc[None, :]
    gram_loc = tdot(obs_c, obs_c)
    cross_loc = tdot(obs_c, row_c)

    size = 128 if obs % 128 == 0 else obs
    nb = obs // size
    pairs = [(i, j) for i in range(nb) for j in range(i + 1)]
    width = -(-(obs + n_rows) // size) * size
    slots = jnp.zeros((n_member, width), jnp.float32)
    slots = lax.dynamic_update_slice(slots, jnp.concatenate([obs_loc, row_loc])[None, :], (me, 0))
    pieces = [gram_loc[i * size:(i + 1) * size, j * size:(j + 1) * size] for i, j in pairs]
    packed = jnp.concatenate(pieces + [slots.reshape(-1, size)], axis=0)
    packed = tree_sum(packed, "member")
    gram_blocks = packed[: len(pairs) * size]
    slots = packed[len(pairs) * size:].reshape(n_member, width)[:, : obs + n_rows]
    cross_loc, gram_blocks, slots = lax.optimization_barrier((cross_loc, gram_blocks, slots))
    cross_sum = tree_sum(cross_loc, "member")

    means = jnp.mean(slots, axis=0)
    dev = slots - means[None, :]
    obs_mean = means[:obs]
    dev_obs = dev[:, :obs]
    dev_row = dev[:, obs:]

    corr = m_loc * tdot(dev_obs, dev_obs)
    blk = [[None] * nb for _ in range(nb)]
    for p, (i, j) in enumerate(pairs):
        part = gram_blocks[p * size:(p + 1) * size] + corr[i * size:(i + 1) * size, j * size:(j + 1) * size]
        part = part / (count - 1.0)
        if i == j:
            part = 0.5 * (part + part.T) + jnp.diag(noise[i * size:(i + 1) * size])
        blk[i][j] = part
    obs_anom = observed - obs_mean[None, :]
    rhs = (target - obs_mean)[:, None] - 0.5 * obs_anom.T
    gain = block_solve(blk, rhs, size)

    cross = (cross_sum + m_loc * tdot(dev_obs, dev_row)) / (count - 1.0)
    return gain, cross


def shards(state, obs_values, noise_var, obs_rows, owner):
    num_blocks = obs_rows.shape[0]
    current = state
    cands = jnp.take(current, obs_rows[0], axis=1)
    for block in range(num_blocks):
        observed = exchange(cands, owner[block])
        gain, cross = analyse(current, observed, obs_values[block], noise_var[block])
        if block + 1 < num_blocks:
            rows = obs_rows[block + 1]
            cands = jnp.take(current, rows, axis=1) + full_dot(gain.T, jnp.take(cross, rows, axis=1))
        current = current + full_dot(gain.T, cross)
    return current


def solution(mesh):
    placed = (P("member", "state"), P(), P(), P(), P())
    return jax.shard_map(
        shards, mesh=mesh, in_specs=placed, out_specs=P("member", "state"), check_vma=False
    )
```

```python
import jax
import jax.numpy as jnp
from jax import lax
from jax.sharding import PartitionSpec as P


def full_dot(left, right):
    return jnp.dot(left, right, precision=lax.Precision.HIGHEST, preferred_element_type=jnp.float32)


def tdot(left, right):
    return lax.dot_general(
        left, right, (((0,), (0,)), ((), ())),
        precision=lax.Precision.HIGHEST, preferred_element_type=jnp.float32,
    )


def _pow2(n):
    return n > 0 and (n & (n - 1)) == 0


def tree_sum(x, axis):
    n = lax.axis_size(axis)
    if n == 1:
        return x
    if not _pow2(n) or x.shape[0] % n != 0:
        return lax.psum(x, axis)
    me = lax.axis_index(axis)
    cur = x
    k = 1
    while k < n:
        perm = [(i, i ^ k) for i in range(n)]
        h = cur.shape[0] // 2
        bit = (me // k) % 2
        keep = lax.dynamic_slice_in_dim(cur, bit * h, h, axis=0)
        away = lax.dynamic_slice_in_dim(cur, (1 - bit) * h, h, axis=0)
        cur = keep + lax.ppermute(away, axis, perm)
        k *= 2
    k = n // 2
    while k >= 1:
        perm = [(i, i ^ k) for i in range(n)]
        bit = (me // k) % 2
        other = lax.ppermute(cur, axis, perm)
        cur = jnp.where(bit == 0, jnp.concatenate([cur, other]), jnp.concatenate([other, cur]))
        k //= 2
    return cur


def tree_sum_exact(x, axis):
    n = lax.axis_size(axis)
    if not _pow2(n):
        return lax.psum(x, axis)
    k = 1
    while k < n:
        perm = [(i, i ^ k) for i in range(n)]
        x = x + lax.ppermute(x, axis, perm)
        k *= 2
    return x


def block_solve(blk, right, size):
    nb = len(blk)
    eye = jnp.eye(size, dtype=right.dtype)
    rhs = [right[i * size:(i + 1) * size] for i in range(nb)]
    low = [[None] * nb for _ in range(nb)]
    inv = [None] * nb
    fwd = [None] * nb
    for k in range(nb):
        diag = lax.linalg.cholesky(blk[k][k], symmetrize_input=False)
        inv[k] = lax.linalg.triangular_solve(diag, eye, left_side=True, lower=True)
        fwd[k] = full_dot(inv[k], rhs[k])
        for i in range(k + 1, nb):
            low[i][k] = full_dot(blk[i][k], inv[k].T)
        for i in range(k + 1, nb):
            for j in range(k + 1, i + 1):
                blk[i][j] = blk[i][j] - full_dot(low[i][k], low[j][k].T)
            rhs[i] = rhs[i] - full_dot(low[i][k], fwd[k])
    out = [None] * nb
    for k in reversed(range(nb)):
        acc = fwd[k]
        for j in range(k + 1, nb):
            acc = acc - tdot(low[j][k], out[j])
        out[k] = tdot(inv[k], acc)
    return jnp.concatenate(out, axis=0)


def exchange(cands, owners_block):
    obs = cands.shape[1]
    tile = obs // owners_block.shape[0]
    own_each = jnp.repeat(owners_block, tile)
    mine = own_each[None, :] == lax.axis_index("state")
    return tree_sum_exact(jnp.where(mine, cands, 0.0), "state")


def analyse(current, observed, target, noise):
    m_loc = current.shape[0]
    n_member = lax.axis_size("member")
    count = m_loc * n_member
    me = lax.axis_index("member")
    n_rows = current.shape[1]
    obs = observed.shape[1]

    row_loc = jnp.mean(current, axis=0)
    obs_loc = jnp.mean(observed, axis=0)
    row_c = current - row_loc[None, :]
    obs_c = observed - obs_loc[None, :]
    gram_loc = tdot(obs_c, obs_c)
    cross_loc = tdot(obs_c, row_c)

    size = 128 if obs % 128 == 0 else obs
    nb = obs // size
    pairs = [(i, j) for i in range(nb) for j in range(i + 1)]
    width = -(-(obs + n_rows) // size) * size
    slots = jnp.zeros((n_member, width), jnp.float32)
    slots = lax.dynamic_update_slice(slots, jnp.concatenate([obs_loc, row_loc])[None, :], (me, 0))
    pieces = [gram_loc[i * size:(i + 1) * size, j * size:(j + 1) * size] for i, j in pairs]
    packed = jnp.concatenate(pieces + [slots.reshape(-1, size)], axis=0)
    packed = tree_sum(packed, "member")
    gram_blocks = packed[: len(pairs) * size]
    slots = packed[len(pairs) * size:].reshape(n_member, width)[:, : obs + n_rows]
    cross_loc, gram_blocks, slots = lax.optimization_barrier((cross_loc, gram_blocks, slots))
    cross_sum = tree_sum(cross_loc, "member")

    means = jnp.mean(slots, axis=0)
    dev = slots - means[None, :]
    obs_mean = means[:obs]
    dev_obs = dev[:, :obs]
    dev_row = dev[:, obs:]

    corr = m_loc * tdot(dev_obs, dev_obs)
    blk = [[None] * nb for _ in range(nb)]
    for p, (i, j) in enumerate(pairs):
        part = gram_blocks[p * size:(p + 1) * size] + corr[i * size:(i + 1) * size, j * size:(j + 1) * size]
        part = part / (count - 1.0)
        if i == j:
            part = 0.5 * (part + part.T) + jnp.diag(noise[i * size:(i + 1) * size])
        blk[i][j] = part
    obs_anom = observed - obs_mean[None, :]
    rhs = (target - obs_mean)[:, None] - 0.5 * obs_anom.T
    gain = block_solve(blk, rhs, size)

    cross = (cross_sum + m_loc * tdot(dev_obs, dev_row)) / (count - 1.0)
    return gain, cross


def serial(state, obs_values, noise_var, obs_rows, owner):
    num_blocks = obs_rows.shape[0]
    current = state
    cands = jnp.take(current, obs_rows[0], axis=1)
    for block in range(num_blocks):
        observed = exchange(cands, owner[block])
        gain, cross = analyse(current, observed, obs_values[block], noise_var[block])
        if block + 1 < num_blocks:
            rows = obs_rows[block + 1]
            cands = jnp.take(current, rows, axis=1) + full_dot(gain.T, jnp.take(cross, rows, axis=1))
        current = current + full_dot(gain.T, cross)
    return current


def lower_blocks(cov, size, noise, count):
    nb = cov.shape[0] // size
    blk = [[None] * nb for _ in range(nb)]
    for i in range(nb):
        for j in range(i + 1):
            part = cov[i * size:(i + 1) * size, j * size:(j + 1) * size] / (count - 1.0)
            if i == j:
                part = 0.5 * (part + part.T) + jnp.diag(noise[i * size:(i + 1) * size])
            blk[i][j] = part
    return blk


def two_blocks(state, obs_values, noise_var, obs_rows, owner):
    m_loc, n_rows = state.shape
    n_member = lax.axis_size("member")
    count = m_loc * n_member
    me = lax.axis_index("member")
    obs = obs_rows.shape[1]
    size = 128 if obs % 128 == 0 else obs

    cands = jnp.concatenate([jnp.take(state, obs_rows[0], axis=1), jnp.take(state, obs_rows[1], axis=1)], axis=1)
    tile = obs // owner.shape[1]
    own_each = jnp.concatenate([jnp.repeat(owner[0], tile), jnp.repeat(owner[1], tile)])
    mine = own_each[None, :] == lax.axis_index("state")
    both = tree_sum_exact(jnp.where(mine, cands, 0.0), "state")

    row_loc = jnp.mean(state, axis=0)
    both_loc = jnp.mean(both, axis=0)
    row_c = state - row_loc[None, :]
    both_c = both - both_loc[None, :]
    gram_loc = tdot(both_c, both_c)
    cross_loc = tdot(both_c[:, :obs], row_c)

    wide = 2 * obs
    nbw = wide // size
    pairs = [(i, j) for i in range(nbw) for j in range(i + 1)]
    width = -(-(wide + n_rows) // size) * size
    slots = jnp.zeros((n_member, width), jnp.float32)
    slots = lax.dynamic_update_slice(slots, jnp.concatenate([both_loc, row_loc])[None, :], (me, 0))
    pieces = [gram_loc[i * size:(i + 1) * size, j * size:(j + 1) * size] for i, j in pairs]
    packed = jnp.concatenate(pieces + [slots.reshape(-1, size)], axis=0)
    packed = tree_sum(packed, "member")
    gram_blocks = packed[: len(pairs) * size]
    slots = packed[len(pairs) * size:].reshape(n_member, width)[:, : wide + n_rows]
    cross_loc, gram_blocks, slots = lax.optimization_barrier((cross_loc, gram_blocks, slots))
    cross_sum = tree_sum(cross_loc, "member")

    means = jnp.mean(slots, axis=0)
    dev = slots - means[None, :]
    dev_both = dev[:, :wide]
    dev_row = dev[:, wide:]
    corr = m_loc * tdot(dev_both, dev_both)
    rows_of = []
    for i in range(nbw):
        cols = []
        for j in range(nbw):
            if j <= i:
                p = pairs.index((i, j))
                part = gram_blocks[p * size:(p + 1) * size]
            else:
                p = pairs.index((j, i))
                part = gram_blocks[p * size:(p + 1) * size].T
            cols.append(part)
        rows_of.append(jnp.concatenate(cols, axis=1))
    moments = jnp.concatenate(rows_of, axis=0) + corr
    gram0 = moments[:obs, :obs]
    zs = moments[:obs, obs:]
    k1 = moments[obs:, obs:]

    mean0 = means[:obs]
    mean1 = means[obs:wide]
    row_mean0 = means[wide:]
    x0 = both[:, :obs]
    x1 = both[:, obs:]

    anom0 = x0 - mean0[None, :]
    d0 = obs_values[0] - mean0
    zp = zs / (count - 1.0)
    rhs0 = jnp.concatenate([d0[:, None] - 0.5 * anom0.T, d0[:, None], zp], axis=1)
    sol0 = block_solve(lower_blocks(gram0, size, noise_var[0], count), rhs0, size)
    gain0 = sol0[:, :m_loc]
    w0 = sol0[:, m_loc]
    wmat = sol0[:, m_loc + 1:]

    cross0 = (cross_sum + m_loc * tdot(dev_both[:, :obs], dev_row)) / (count - 1.0)
    current1 = state + full_dot(gain0.T, cross0)

    row_mean1 = row_mean0 + full_dot(w0[None, :], cross0)[0]
    mean1 = mean1 + full_dot(w0[None, :], zp)[0]
    x1 = x1 + full_dot(gain0.T, zp)
    gram1 = k1 - tdot(zs, wmat) + 0.25 * tdot(wmat, full_dot(gram0, wmat))
    anom1 = x1 - mean1[None, :]
    d1 = obs_values[1] - mean1
    rhs1 = d1[:, None] - 0.5 * anom1.T
    gain1 = block_solve(lower_blocks(gram1, size, noise_var[1], count), rhs1, size)
    cross1_loc = tdot(anom1, current1 - row_mean1[None, :])
    cross1 = tree_sum(cross1_loc, "member") / (count - 1.0)
    return current1 + full_dot(gain1.T, cross1)


def shards(state, obs_values, noise_var, obs_rows, owner):
    if obs_rows.shape[0] == 2:
        return two_blocks(state, obs_values, noise_var, obs_rows, owner)
    return serial(state, obs_values, noise_var, obs_rows, owner)


def solution(mesh):
    placed = (P("member", "state"), P(), P(), P(), P())
    return jax.shard_map(
        shards, mesh=mesh, in_specs=placed, out_specs=P("member", "state"), check_vma=False
    )
```

```python
import jax
import jax.numpy as jnp
from jax import lax
from jax.sharding import PartitionSpec as P


def full_dot(left, right):
    return jnp.dot(left, right, precision=lax.Precision.HIGHEST, preferred_element_type=jnp.float32)


def tdot(left, right):
    return lax.dot_general(
        left, right, (((0,), (0,)), ((), ())),
        precision=lax.Precision.HIGHEST, preferred_element_type=jnp.float32,
    )


def _pow2(n):
    return n > 0 and (n & (n - 1)) == 0


def tree_sum(x, axis):
    n = lax.axis_size(axis)
    if n == 1:
        return x
    if not _pow2(n) or x.shape[0] % n != 0:
        return lax.psum(x, axis)
    me = lax.axis_index(axis)
    cur = x
    k = 1
    while k < n:
        perm = [(i, i ^ k) for i in range(n)]
        h = cur.shape[0] // 2
        bit = (me // k) % 2
        keep = lax.dynamic_slice_in_dim(cur, bit * h, h, axis=0)
        away = lax.dynamic_slice_in_dim(cur, (1 - bit) * h, h, axis=0)
        cur = keep + lax.ppermute(away, axis, perm)
        k *= 2
    k = n // 2
    while k >= 1:
        perm = [(i, i ^ k) for i in range(n)]
        bit = (me // k) % 2
        other = lax.ppermute(cur, axis, perm)
        cur = jnp.where(bit == 0, jnp.concatenate([cur, other]), jnp.concatenate([other, cur]))
        k //= 2
    return cur


def tree_sum_exact(x, axis):
    n = lax.axis_size(axis)
    if not _pow2(n):
        return lax.psum(x, axis)
    k = 1
    while k < n:
        perm = [(i, i ^ k) for i in range(n)]
        x = x + lax.ppermute(x, axis, perm)
        k *= 2
    return x


def block_solve(blk, right, size):
    nb = len(blk)
    eye = jnp.eye(size, dtype=right.dtype)
    rhs = [right[i * size:(i + 1) * size] for i in range(nb)]
    low = [[None] * nb for _ in range(nb)]
    inv = [None] * nb
    fwd = [None] * nb
    for k in range(nb):
        diag = lax.linalg.cholesky(blk[k][k], symmetrize_input=False)
        inv[k] = lax.linalg.triangular_solve(diag, eye, left_side=True, lower=True)
        fwd[k] = full_dot(inv[k], rhs[k])
        for i in range(k + 1, nb):
            low[i][k] = full_dot(blk[i][k], inv[k].T)
        for i in range(k + 1, nb):
            for j in range(k + 1, i + 1):
                blk[i][j] = blk[i][j] - full_dot(low[i][k], low[j][k].T)
            rhs[i] = rhs[i] - full_dot(low[i][k], fwd[k])
    out = [None] * nb
    for k in reversed(range(nb)):
        acc = fwd[k]
        for j in range(k + 1, nb):
            acc = acc - tdot(low[j][k], out[j])
        out[k] = tdot(inv[k], acc)
    return jnp.concatenate(out, axis=0)


def exchange(cands, owners_block):
    obs = cands.shape[1]
    tile = obs // owners_block.shape[0]
    own_each = jnp.repeat(owners_block, tile)
    mine = own_each[None, :] == lax.axis_index("state")
    return tree_sum_exact(jnp.where(mine, cands, 0.0), "state")


def analyse(current, observed, target, noise):
    m_loc = current.shape[0]
    n_member = lax.axis_size("member")
    count = m_loc * n_member
    me = lax.axis_index("member")
    n_rows = current.shape[1]
    obs = observed.shape[1]

    row_loc = jnp.mean(current, axis=0)
    obs_loc = jnp.mean(observed, axis=0)
    row_c = current - row_loc[None, :]
    obs_c = observed - obs_loc[None, :]
    gram_loc = tdot(obs_c, obs_c)
    cross_loc = tdot(obs_c, row_c)

    size = 128 if obs % 128 == 0 else obs
    nb = obs // size
    pairs = [(i, j) for i in range(nb) for j in range(i + 1)]
    width = -(-(obs + n_rows) // size) * size
    slots = jnp.zeros((n_member, width), jnp.float32)
    slots = lax.dynamic_update_slice(slots, jnp.concatenate([obs_loc, row_loc])[None, :], (me, 0))
    pieces = [gram_loc[i * size:(i + 1) * size, j * size:(j + 1) * size] for i, j in pairs]
    n_gram = len(pairs) * size
    n_slot = n_member * width // size
    cross_pad = -(-n_rows // size) * size
    cross_wide = jnp.pad(cross_loc, ((0, 0), (0, cross_pad - n_rows)))
    cross_parts = [cross_wide[:, c * size:(c + 1) * size] for c in range(cross_pad // size)]
    packed = jnp.concatenate(pieces + [slots.reshape(-1, size)] + cross_parts, axis=0)
    packed = tree_sum(packed, "member")
    gram_blocks = packed[:n_gram]
    slots = packed[n_gram:n_gram + n_slot].reshape(n_member, width)[:, : obs + n_rows]
    tail = packed[n_gram + n_slot:]
    cross_sum = jnp.concatenate(
        [tail[c * obs:(c + 1) * obs] for c in range(cross_pad // size)], axis=1
    )[:, :n_rows]

    means = jnp.mean(slots, axis=0)
    dev = slots - means[None, :]
    obs_mean = means[:obs]
    dev_obs = dev[:, :obs]
    dev_row = dev[:, obs:]

    corr = m_loc * tdot(dev_obs, dev_obs)
    blk = [[None] * nb for _ in range(nb)]
    for p, (i, j) in enumerate(pairs):
        part = gram_blocks[p * size:(p + 1) * size] + corr[i * size:(i + 1) * size, j * size:(j + 1) * size]
        part = part / (count - 1.0)
        if i == j:
            part = 0.5 * (part + part.T) + jnp.diag(noise[i * size:(i + 1) * size])
        blk[i][j] = part
    obs_anom = observed - obs_mean[None, :]
    rhs = (target - obs_mean)[:, None] - 0.5 * obs_anom.T
    gain = block_solve(blk, rhs, size)

    cross = (cross_sum + m_loc * tdot(dev_obs, dev_row)) / (count - 1.0)
    return gain, cross


def shards(state, obs_values, noise_var, obs_rows, owner):
    num_blocks = obs_rows.shape[0]
    current = state
    cands = jnp.take(current, obs_rows[0], axis=1)
    for block in range(num_blocks):
        observed = exchange(cands, owner[block])
        gain, cross = analyse(current, observed, obs_values[block], noise_var[block])
        if block + 1 < num_blocks:
            rows = obs_rows[block + 1]
            cands = jnp.take(current, rows, axis=1) + full_dot(gain.T, jnp.take(cross, rows, axis=1))
        current = current + full_dot(gain.T, cross)
    return current


def solution(mesh):
    placed = (P("member", "state"), P(), P(), P(), P())
    return jax.shard_map(
        shards, mesh=mesh, in_specs=placed, out_specs=P("member", "state"), check_vma=False
    )
```

```python
import jax
import jax.numpy as jnp
from jax import lax
from jax.sharding import PartitionSpec as P


def full_dot(left, right):
    return jnp.dot(left, right, precision=lax.Precision.HIGHEST, preferred_element_type=jnp.float32)


def tdot(left, right):
    return lax.dot_general(
        left, right, (((0,), (0,)), ((), ())),
        precision=lax.Precision.HIGHEST, preferred_element_type=jnp.float32,
    )


def _pow2(n):
    return n > 0 and (n & (n - 1)) == 0


def tree_sum(x, axis):
    n = lax.axis_size(axis)
    if n == 1:
        return x
    if not _pow2(n) or x.shape[0] % n != 0:
        return lax.psum(x, axis)
    me = lax.axis_index(axis)
    cur = x
    k = 1
    while k < n:
        perm = [(i, i ^ k) for i in range(n)]
        h = cur.shape[0] // 2
        bit = (me // k) % 2
        keep = lax.dynamic_slice_in_dim(cur, bit * h, h, axis=0)
        away = lax.dynamic_slice_in_dim(cur, (1 - bit) * h, h, axis=0)
        cur = keep + lax.ppermute(away, axis, perm)
        k *= 2
    k = n // 2
    while k >= 1:
        perm = [(i, i ^ k) for i in range(n)]
        bit = (me // k) % 2
        other = lax.ppermute(cur, axis, perm)
        cur = jnp.where(bit == 0, jnp.concatenate([cur, other]), jnp.concatenate([other, cur]))
        k //= 2
    return cur


def tree_sum_exact(x, axis):
    n = lax.axis_size(axis)
    if not _pow2(n):
        return lax.psum(x, axis)
    k = 1
    while k < n:
        perm = [(i, i ^ k) for i in range(n)]
        x = x + lax.ppermute(x, axis, perm)
        k *= 2
    return x


def block_solve(blk, right, size):
    nb = len(blk)
    eye = jnp.eye(size, dtype=right.dtype)
    rhs = [right[i * size:(i + 1) * size] for i in range(nb)]
    low = [[None] * nb for _ in range(nb)]
    inv = [None] * nb
    fwd = [None] * nb
    for k in range(nb):
        diag = lax.linalg.cholesky(blk[k][k], symmetrize_input=False)
        inv[k] = lax.linalg.triangular_solve(diag, eye, left_side=True, lower=True)
        fwd[k] = full_dot(inv[k], rhs[k])
        for i in range(k + 1, nb):
            low[i][k] = full_dot(blk[i][k], inv[k].T)
        for i in range(k + 1, nb):
            for j in range(k + 1, i + 1):
                blk[i][j] = blk[i][j] - full_dot(low[i][k], low[j][k].T)
            rhs[i] = rhs[i] - full_dot(low[i][k], fwd[k])
    out = [None] * nb
    for k in reversed(range(nb)):
        acc = fwd[k]
        for j in range(k + 1, nb):
            acc = acc - tdot(low[j][k], out[j])
        out[k] = tdot(inv[k], acc)
    return jnp.concatenate(out, axis=0)


def exchange(cands, owners_block):
    obs = cands.shape[1]
    tile = obs // owners_block.shape[0]
    own_each = jnp.repeat(owners_block, tile)
    mine = own_each[None, :] == lax.axis_index("state")
    return tree_sum_exact(jnp.where(mine, cands, 0.0), "state")


def analyse(current, observed, target, noise):
    m_loc = current.shape[0]
    n_member = lax.axis_size("member")
    count = m_loc * n_member
    me = lax.axis_index("member")
    n_rows = current.shape[1]
    obs = observed.shape[1]

    row_loc = jnp.mean(current, axis=0)
    obs_loc = jnp.mean(observed, axis=0)
    row_c = current - row_loc[None, :]
    obs_c = observed - obs_loc[None, :]
    gram_loc = tdot(obs_c, obs_c)
    cross_loc = tdot(obs_c, row_c)

    size = 128 if obs % 128 == 0 else obs
    nb = obs // size
    pairs = [(i, j) for i in range(nb) for j in range(i + 1)]
    width = -(-(obs + n_rows) // size) * size
    slots = jnp.zeros((n_member, width), jnp.float32)
    slots = lax.dynamic_update_slice(slots, jnp.concatenate([obs_loc, row_loc])[None, :], (me, 0))
    pieces = [gram_loc[i * size:(i + 1) * size, j * size:(j + 1) * size] for i, j in pairs]
    packed = jnp.concatenate(pieces + [slots.reshape(-1, size)], axis=0)
    packed = tree_sum(packed, "member")
    gram_blocks = packed[: len(pairs) * size]
    slots = packed[len(pairs) * size:].reshape(n_member, width)[:, : obs + n_rows]
    cross_loc, gram_blocks, slots = lax.optimization_barrier((cross_loc, gram_blocks, slots))
    cross_sum = tree_sum(cross_loc, "member")

    means = jnp.mean(slots, axis=0)
    dev = slots - means[None, :]
    obs_mean = means[:obs]
    dev_obs = dev[:, :obs]
    dev_row = dev[:, obs:]

    corr = m_loc * tdot(dev_obs, dev_obs)
    blk = [[None] * nb for _ in range(nb)]
    for p, (i, j) in enumerate(pairs):
        part = gram_blocks[p * size:(p + 1) * size] + corr[i * size:(i + 1) * size, j * size:(j + 1) * size]
        part = part / (count - 1.0)
        if i == j:
            part = 0.5 * (part + part.T) + jnp.diag(noise[i * size:(i + 1) * size])
        blk[i][j] = part
    obs_anom = observed - obs_mean[None, :]
    rhs = (target - obs_mean)[:, None] - 0.5 * obs_anom.T
    gain = block_solve(blk, rhs, size)

    cross = (cross_sum + m_loc * tdot(dev_obs, dev_row)) / (count - 1.0)
    return gain, cross


def shards(state, obs_values, noise_var, obs_rows, owner):
    num_blocks = obs_rows.shape[0]
    current = state
    cands = jnp.take(current, obs_rows[0], axis=1)
    for block in range(num_blocks):
        observed = exchange(cands, owner[block])
        gain, cross = analyse(current, observed, obs_values[block], noise_var[block])
        if block + 1 < num_blocks:
            rows = obs_rows[block + 1]
            picked = jnp.take(current, rows, axis=1)
            cands = picked + full_dot(gain.T, jnp.take(cross, rows, axis=1))
        current = current + full_dot(gain.T, cross)
    return current


def solution(mesh):
    placed = (P("member", "state"), P(), P(), P(), P())
    return jax.shard_map(
        shards, mesh=mesh, in_specs=placed, out_specs=P("member", "state"), check_vma=False
    )
```

```python
import jax
import jax.numpy as jnp
from jax import lax
from jax.sharding import PartitionSpec as P


def full_dot(left, right):
    return jnp.dot(left, right, precision=lax.Precision.HIGHEST, preferred_element_type=jnp.float32)


def tdot(left, right):
    return lax.dot_general(
        left, right, (((0,), (0,)), ((), ())),
        precision=lax.Precision.HIGHEST, preferred_element_type=jnp.float32,
    )


def _pow2(n):
    return n > 0 and (n & (n - 1)) == 0


def tree_sum(x, axis):
    n = lax.axis_size(axis)
    if n == 1:
        return x
    if not _pow2(n) or x.shape[0] % n != 0:
        return lax.psum(x, axis)
    me = lax.axis_index(axis)
    cur = x
    k = 1
    while k < n:
        perm = [(i, i ^ k) for i in range(n)]
        h = cur.shape[0] // 2
        bit = (me // k) % 2
        keep = lax.dynamic_slice_in_dim(cur, bit * h, h, axis=0)
        away = lax.dynamic_slice_in_dim(cur, (1 - bit) * h, h, axis=0)
        cur = keep + lax.ppermute(away, axis, perm)
        k *= 2
    k = n // 2
    while k >= 1:
        perm = [(i, i ^ k) for i in range(n)]
        bit = (me // k) % 2
        other = lax.ppermute(cur, axis, perm)
        cur = jnp.where(bit == 0, jnp.concatenate([cur, other]), jnp.concatenate([other, cur]))
        k //= 2
    return cur


def tree_sum_exact(x, axis):
    n = lax.axis_size(axis)
    if not _pow2(n):
        return lax.psum(x, axis)
    k = 1
    while k < n:
        perm = [(i, i ^ k) for i in range(n)]
        x = x + lax.ppermute(x, axis, perm)
        k *= 2
    return x


def block_solve(blk, right, size):
    nb = len(blk)
    eye = jnp.eye(size, dtype=right.dtype)
    rhs = [right[i * size:(i + 1) * size] for i in range(nb)]
    low = [[None] * nb for _ in range(nb)]
    inv = [None] * nb
    fwd = [None] * nb
    for k in range(nb):
        diag = lax.linalg.cholesky(blk[k][k], symmetrize_input=False)
        inv[k] = lax.linalg.triangular_solve(diag, eye, left_side=True, lower=True)
        fwd[k] = full_dot(inv[k], rhs[k])
        for i in range(k + 1, nb):
            low[i][k] = full_dot(blk[i][k], inv[k].T)
        for i in range(k + 1, nb):
            for j in range(k + 1, i + 1):
                blk[i][j] = blk[i][j] - full_dot(low[i][k], low[j][k].T)
            rhs[i] = rhs[i] - full_dot(low[i][k], fwd[k])
    out = [None] * nb
    for k in reversed(range(nb)):
        acc = fwd[k]
        for j in range(k + 1, nb):
            acc = acc - tdot(low[j][k], out[j])
        out[k] = tdot(inv[k], acc)
    return jnp.concatenate(out, axis=0)


def exchange(cands, owners_block):
    obs = cands.shape[1]
    tile = obs // owners_block.shape[0]
    own_each = jnp.repeat(owners_block, tile)
    mine = own_each[None, :] == lax.axis_index("state")
    return tree_sum_exact(jnp.where(mine, cands, 0.0), "state")


def analyse(current, observed, target, noise):
    m_loc = current.shape[0]
    n_member = lax.axis_size("member")
    count = m_loc * n_member
    me = lax.axis_index("member")
    n_rows = current.shape[1]
    obs = observed.shape[1]

    row_loc = jnp.mean(current, axis=0)
    obs_loc = jnp.mean(observed, axis=0)
    row_c = current - row_loc[None, :]
    obs_c = observed - obs_loc[None, :]
    gram_loc = tdot(obs_c, obs_c)
    cross_loc = tdot(obs_c, row_c)

    size = 128 if obs % 128 == 0 else obs
    nb = obs // size
    pairs = [(i, j) for i in range(nb) for j in range(i + 1)]
    width = -(-(obs + n_rows) // size) * size
    slots = jnp.zeros((n_member, width), jnp.float32)
    slots = lax.dynamic_update_slice(slots, jnp.concatenate([obs_loc, row_loc])[None, :], (me, 0))
    pieces = [gram_loc[i * size:(i + 1) * size, j * size:(j + 1) * size] for i, j in pairs]
    packed = jnp.concatenate(pieces + [slots.reshape(-1, size)], axis=0)
    packed = tree_sum(packed, "member")
    gram_blocks = packed[: len(pairs) * size]
    slots = packed[len(pairs) * size:].reshape(n_member, width)[:, : obs + n_rows]
    cross_loc, gram_blocks, slots = lax.optimization_barrier((cross_loc, gram_blocks, slots))
    cross_sum = tree_sum(cross_loc, "member")

    means = jnp.mean(slots, axis=0)
    dev = slots - means[None, :]
    obs_mean = means[:obs]
    dev_obs = dev[:, :obs]
    dev_row = dev[:, obs:]

    corr = m_loc * tdot(dev_obs, dev_obs)
    blk = [[None] * nb for _ in range(nb)]
    for p, (i, j) in enumerate(pairs):
        part = gram_blocks[p * size:(p + 1) * size] + corr[i * size:(i + 1) * size, j * size:(j + 1) * size]
        part = part / (count - 1.0)
        if i == j:
            part = part + jnp.eye(size, dtype=part.dtype) * noise[i * size:(i + 1) * size][None, :]
        blk[i][j] = part
    obs_anom = observed - obs_mean[None, :]
    rhs = (target - obs_mean)[:, None] - 0.5 * obs_anom.T
    gain = block_solve(blk, rhs, size)

    cross = (cross_sum + m_loc * tdot(dev_obs, dev_row)) / (count - 1.0)
    return gain, cross


def shards(state, obs_values, noise_var, obs_rows, owner):
    num_blocks = obs_rows.shape[0]
    current = state
    cands = jnp.take(current, obs_rows[0], axis=1)
    for block in range(num_blocks):
        observed = exchange(cands, owner[block])
        gain, cross = analyse(current, observed, obs_values[block], noise_var[block])
        if block + 1 < num_blocks:
            rows = obs_rows[block + 1]
            cands = jnp.take(current, rows, axis=1) + full_dot(gain.T, jnp.take(cross, rows, axis=1))
        current = current + full_dot(gain.T, cross)
    return current


def solution(mesh):
    placed = (P("member", "state"), P(), P(), P(), P())
    return jax.shard_map(
        shards, mesh=mesh, in_specs=placed, out_specs=P("member", "state"), check_vma=False
    )
```

```python
import jax
import jax.numpy as jnp
from jax import lax
from jax.sharding import PartitionSpec as P


def full_dot(left, right):
    return jnp.dot(left, right, precision=lax.Precision.HIGHEST, preferred_element_type=jnp.float32)


def tdot(left, right):
    return lax.dot_general(
        left, right, (((0,), (0,)), ((), ())),
        precision=lax.Precision.HIGHEST, preferred_element_type=jnp.float32,
    )


def _pow2(n):
    return n > 0 and (n & (n - 1)) == 0


def tree_sum(x, axis):
    n = lax.axis_size(axis)
    if n == 1:
        return x
    if not _pow2(n) or x.shape[0] % n != 0:
        return lax.psum(x, axis)
    me = lax.axis_index(axis)
    cur = x
    k = 1
    while k < n:
        perm = [(i, i ^ k) for i in range(n)]
        h = cur.shape[0] // 2
        bit = (me // k) % 2
        keep = lax.dynamic_slice_in_dim(cur, bit * h, h, axis=0)
        away = lax.dynamic_slice_in_dim(cur, (1 - bit) * h, h, axis=0)
        cur = keep + lax.ppermute(away, axis, perm)
        k *= 2
    k = n // 2
    while k >= 1:
        perm = [(i, i ^ k) for i in range(n)]
        bit = (me // k) % 2
        other = lax.ppermute(cur, axis, perm)
        cur = jnp.where(bit == 0, jnp.concatenate([cur, other]), jnp.concatenate([other, cur]))
        k //= 2
    return cur


def tree_sum_exact(x, axis):
    n = lax.axis_size(axis)
    if not _pow2(n):
        return lax.psum(x, axis)
    k = 1
    while k < n:
        perm = [(i, i ^ k) for i in range(n)]
        x = x + lax.ppermute(x, axis, perm)
        k *= 2
    return x


def block_solve(blk, right, size):
    nb = len(blk)
    eye = jnp.eye(size, dtype=right.dtype)
    rhs = [right[i * size:(i + 1) * size] for i in range(nb)]
    low = [[None] * nb for _ in range(nb)]
    inv = [None] * nb
    fwd = [None] * nb
    for k in range(nb):
        diag = lax.linalg.cholesky(blk[k][k], symmetrize_input=False)
        inv[k] = lax.linalg.triangular_solve(diag, eye, left_side=True, lower=True)
        fwd[k] = full_dot(inv[k], rhs[k])
        for i in range(k + 1, nb):
            low[i][k] = full_dot(blk[i][k], inv[k].T)
        for i in range(k + 1, nb):
            for j in range(k + 1, i + 1):
                blk[i][j] = blk[i][j] - full_dot(low[i][k], low[j][k].T)
            rhs[i] = rhs[i] - full_dot(low[i][k], fwd[k])
    out = [None] * nb
    for k in reversed(range(nb)):
        acc = fwd[k]
        for j in range(k + 1, nb):
            acc = acc - tdot(low[j][k], out[j])
        out[k] = tdot(inv[k], acc)
    return jnp.concatenate(out, axis=0)


def exchange(cands, owners_block):
    obs = cands.shape[1]
    tile = obs // owners_block.shape[0]
    own_each = jnp.repeat(owners_block, tile)
    mine = own_each[None, :] == lax.axis_index("state")
    return tree_sum_exact(jnp.where(mine, cands, 0.0), "state")


def analyse(current, observed, target, noise):
    m_loc = current.shape[0]
    n_member = lax.axis_size("member")
    count = m_loc * n_member
    me = lax.axis_index("member")
    n_rows = current.shape[1]
    obs = observed.shape[1]

    row_loc = jnp.mean(current, axis=0)
    obs_loc = jnp.mean(observed, axis=0)
    row_c = current - row_loc[None, :]
    obs_c = observed - obs_loc[None, :]
    gram_loc = tdot(obs_c, obs_c)
    cross_loc = tdot(obs_c, row_c)

    size = 128 if obs % 128 == 0 else obs
    nb = obs // size
    pairs = [(i, j) for i in range(nb) for j in range(i + 1)]
    width = -(-(obs + n_rows) // size) * size
    slots = jnp.zeros((n_member, width), jnp.float32)
    slots = lax.dynamic_update_slice(slots, jnp.concatenate([obs_loc, row_loc])[None, :], (me, 0))
    pieces = [gram_loc[i * size:(i + 1) * size, j * size:(j + 1) * size] for i, j in pairs]
    packed = jnp.concatenate(pieces + [slots.reshape(-1, size)], axis=0)
    packed = tree_sum(packed, "member")
    gram_blocks = packed[: len(pairs) * size]
    slots = packed[len(pairs) * size:].reshape(n_member, width)[:, : obs + n_rows]
    cross_sum = tree_sum(cross_loc, "member")

    means = jnp.mean(slots, axis=0)
    dev = slots - means[None, :]
    obs_mean = means[:obs]
    dev_obs = dev[:, :obs]
    dev_row = dev[:, obs:]

    corr = m_loc * tdot(dev_obs, dev_obs)
    blk = [[None] * nb for _ in range(nb)]
    for p, (i, j) in enumerate(pairs):
        part = gram_blocks[p * size:(p + 1) * size] + corr[i * size:(i + 1) * size, j * size:(j + 1) * size]
        part = part / (count - 1.0)
        if i == j:
            part = part + jnp.eye(size, dtype=part.dtype) * noise[i * size:(i + 1) * size][None, :]
        blk[i][j] = part
    obs_anom = observed - obs_mean[None, :]
    rhs = (target - obs_mean)[:, None] - 0.5 * obs_anom.T
    shift = lax.optimization_barrier(m_loc * tdot(dev_obs, dev_row) / (count - 1.0))
    gain = block_solve(blk, rhs, size)

    cross = cross_sum / (count - 1.0) + shift
    return gain, cross


def shards(state, obs_values, noise_var, obs_rows, owner):
    num_blocks = obs_rows.shape[0]
    current = state
    cands = jnp.take(current, obs_rows[0], axis=1)
    for block in range(num_blocks):
        observed = exchange(cands, owner[block])
        gain, cross = analyse(current, observed, obs_values[block], noise_var[block])
        if block + 1 < num_blocks:
            rows = obs_rows[block + 1]
            picked = jnp.take(current, rows, axis=1)
            cands = picked + full_dot(gain.T, jnp.take(cross, rows, axis=1))
        current = current + full_dot(gain.T, cross)
    return current


def solution(mesh):
    placed = (P("member", "state"), P(), P(), P(), P())
    return jax.shard_map(
        shards, mesh=mesh, in_specs=placed, out_specs=P("member", "state"), check_vma=False
    )
```

```python
import jax
import jax.numpy as jnp
from jax import lax
from jax.sharding import PartitionSpec as P


def full_dot(left, right):
    return jnp.dot(left, right, precision=lax.Precision.HIGHEST, preferred_element_type=jnp.float32)


def tdot(left, right):
    return lax.dot_general(
        left, right, (((0,), (0,)), ((), ())),
        precision=lax.Precision.HIGHEST, preferred_element_type=jnp.float32,
    )


def _pow2(n):
    return n > 0 and (n & (n - 1)) == 0


def tree_sum(x, axis):
    n = lax.axis_size(axis)
    if n == 1:
        return x
    if not _pow2(n) or x.shape[0] % n != 0:
        return lax.psum(x, axis)
    me = lax.axis_index(axis)
    cur = x
    k = 1
    while k < n:
        perm = [(i, i ^ k) for i in range(n)]
        h = cur.shape[0] // 2
        bit = (me // k) % 2
        keep = lax.dynamic_slice_in_dim(cur, bit * h, h, axis=0)
        away = lax.dynamic_slice_in_dim(cur, (1 - bit) * h, h, axis=0)
        cur = keep + lax.ppermute(away, axis, perm)
        k *= 2
    k = n // 2
    while k >= 1:
        perm = [(i, i ^ k) for i in range(n)]
        bit = (me // k) % 2
        other = lax.ppermute(cur, axis, perm)
        cur = jnp.where(bit == 0, jnp.concatenate([cur, other]), jnp.concatenate([other, cur]))
        k //= 2
    return cur


def tree_sum_exact(x, axis):
    n = lax.axis_size(axis)
    if not _pow2(n):
        return lax.psum(x, axis)
    k = 1
    while k < n:
        perm = [(i, i ^ k) for i in range(n)]
        x = x + lax.ppermute(x, axis, perm)
        k *= 2
    return x


def block_solve(blk, right, size):
    nb = len(blk)
    eye = jnp.eye(size, dtype=right.dtype)
    rhs = [right[i * size:(i + 1) * size] for i in range(nb)]
    low = [[None] * nb for _ in range(nb)]
    inv = [None] * nb
    fwd = [None] * nb
    for k in range(nb):
        diag = lax.linalg.cholesky(blk[k][k], symmetrize_input=False)
        inv[k] = lax.linalg.triangular_solve(diag, eye, left_side=True, lower=True)
        fwd[k] = full_dot(inv[k], rhs[k])
        for i in range(k + 1, nb):
            low[i][k] = full_dot(blk[i][k], inv[k].T)
        for i in range(k + 1, nb):
            for j in range(k + 1, i + 1):
                blk[i][j] = blk[i][j] - full_dot(low[i][k], low[j][k].T)
            rhs[i] = rhs[i] - full_dot(low[i][k], fwd[k])
    out = [None] * nb
    for k in reversed(range(nb)):
        acc = fwd[k]
        for j in range(k + 1, nb):
            acc = acc - tdot(low[j][k], out[j])
        out[k] = tdot(inv[k], acc)
    return jnp.concatenate(out, axis=0)


def exchange(cands, owners_block):
    obs = cands.shape[1]
    tile = obs // owners_block.shape[0]
    own_each = jnp.repeat(owners_block, tile)
    mine = own_each[None, :] == lax.axis_index("state")
    return tree_sum_exact(jnp.where(mine, cands, 0.0), "state")


def analyse(current, observed, target, noise):
    m_loc = current.shape[0]
    n_member = lax.axis_size("member")
    count = m_loc * n_member
    me = lax.axis_index("member")
    n_rows = current.shape[1]
    obs = observed.shape[1]

    row_loc = jnp.mean(current, axis=0)
    obs_loc = jnp.mean(observed, axis=0)
    row_c = current - row_loc[None, :]
    obs_c = observed - obs_loc[None, :]
    gram_loc = tdot(obs_c, obs_c)
    cross_loc = tdot(obs_c, row_c)

    size = 128 if obs % 128 == 0 else obs
    nb = obs // size
    pairs = [(i, j) for i in range(nb) for j in range(i + 1)]
    width = -(-(obs + n_rows) // size) * size
    slots = jnp.zeros((n_member, width), jnp.float32)
    slots = lax.dynamic_update_slice(slots, jnp.concatenate([obs_loc, row_loc])[None, :], (me, 0))
    pieces = [gram_loc[i * size:(i + 1) * size, j * size:(j + 1) * size] for i, j in pairs]
    packed = jnp.concatenate(pieces + [slots.reshape(-1, size)], axis=0)
    packed = tree_sum(packed, "member")
    gram_blocks = packed[: len(pairs) * size]
    slots = packed[len(pairs) * size:].reshape(n_member, width)[:, : obs + n_rows]
    cross_sum = tree_sum(cross_loc, "member")

    means = jnp.mean(slots, axis=0)
    dev = slots - means[None, :]
    obs_mean = means[:obs]
    dev_obs = dev[:, :obs]
    dev_row = dev[:, obs:]

    corr = m_loc * tdot(dev_obs, dev_obs)
    blk = [[None] * nb for _ in range(nb)]
    for p, (i, j) in enumerate(pairs):
        part = gram_blocks[p * size:(p + 1) * size] + corr[i * size:(i + 1) * size, j * size:(j + 1) * size]
        part = part / (count - 1.0)
        if i == j:
            part = part + jnp.eye(size, dtype=part.dtype) * noise[i * size:(i + 1) * size][None, :]
        blk[i][j] = part
    obs_anom = observed - obs_mean[None, :]
    rhs = (target - obs_mean)[:, None] - 0.5 * obs_anom.T
    gain = block_solve(blk, rhs, size)

    cross = (cross_sum + m_loc * tdot(dev_obs, dev_row)) / (count - 1.0)
    return gain, cross


def shards(state, obs_values, noise_var, obs_rows, owner):
    num_blocks = obs_rows.shape[0]
    current = state
    cands = jnp.take(current, obs_rows[0], axis=1)
    for block in range(num_blocks):
        observed = exchange(cands, owner[block])
        gain, cross = analyse(current, observed, obs_values[block], noise_var[block])
        if block + 1 < num_blocks:
            rows = obs_rows[block + 1]
            picked = jnp.take(current, rows, axis=1)
        step = full_dot(gain.T, cross)
        if block + 1 < num_blocks:
            cands = picked + jnp.take(step, rows, axis=1)
        current = current + step
    return current


def solution(mesh):
    placed = (P("member", "state"), P(), P(), P(), P())
    return jax.shard_map(
        shards, mesh=mesh, in_specs=placed, out_specs=P("member", "state"), check_vma=False
    )
```

```python
import jax
import jax.numpy as jnp
from jax import lax
from jax.sharding import PartitionSpec as P


def full_dot(left, right):
    return jnp.dot(left, right, precision=lax.Precision.HIGHEST, preferred_element_type=jnp.float32)


def tdot(left, right):
    return lax.dot_general(
        left, right, (((0,), (0,)), ((), ())),
        precision=lax.Precision.HIGHEST, preferred_element_type=jnp.float32,
    )


def _pow2(n):
    return n > 0 and (n & (n - 1)) == 0


def tree_sum(x, axis):
    n = lax.axis_size(axis)
    if n == 1:
        return x
    if not _pow2(n) or x.shape[0] % n != 0:
        return lax.psum(x, axis)
    me = lax.axis_index(axis)
    cur = x
    k = 1
    while k < n:
        perm = [(i, i ^ k) for i in range(n)]
        h = cur.shape[0] // 2
        bit = (me // k) % 2
        keep = lax.dynamic_slice_in_dim(cur, bit * h, h, axis=0)
        away = lax.dynamic_slice_in_dim(cur, (1 - bit) * h, h, axis=0)
        cur = keep + lax.ppermute(away, axis, perm)
        k *= 2
    k = n // 2
    while k >= 1:
        perm = [(i, i ^ k) for i in range(n)]
        bit = (me // k) % 2
        other = lax.ppermute(cur, axis, perm)
        cur = jnp.where(bit == 0, jnp.concatenate([cur, other]), jnp.concatenate([other, cur]))
        k //= 2
    return cur


def tree_sum_exact(x, axis):
    n = lax.axis_size(axis)
    if not _pow2(n):
        return lax.psum(x, axis)
    k = 1
    while k < n:
        perm = [(i, i ^ k) for i in range(n)]
        x = x + lax.ppermute(x, axis, perm)
        k *= 2
    return x


def block_solve(blk, right, size):
    nb = len(blk)
    eye = jnp.eye(size, dtype=right.dtype)
    rhs = [right[i * size:(i + 1) * size] for i in range(nb)]
    low = [[None] * nb for _ in range(nb)]
    inv = [None] * nb
    fwd = [None] * nb
    for k in range(nb):
        diag = lax.linalg.cholesky(blk[k][k], symmetrize_input=False)
        inv[k] = lax.linalg.triangular_solve(diag, eye, left_side=True, lower=True)
        fwd[k] = full_dot(inv[k], rhs[k])
        for i in range(k + 1, nb):
            low[i][k] = full_dot(blk[i][k], inv[k].T)
        for i in range(k + 1, nb):
            for j in range(k + 1, i + 1):
                blk[i][j] = blk[i][j] - full_dot(low[i][k], low[j][k].T)
            rhs[i] = rhs[i] - full_dot(low[i][k], fwd[k])
    out = [None] * nb
    for k in reversed(range(nb)):
        acc = fwd[k]
        for j in range(k + 1, nb):
            acc = acc - tdot(low[j][k], out[j])
        out[k] = tdot(inv[k], acc)
    return jnp.concatenate(out, axis=0)


def exchange(cands, owners_block):
    obs = cands.shape[1]
    tile = obs // owners_block.shape[0]
    own_each = jnp.repeat(owners_block, tile)
    mine = own_each[None, :] == lax.axis_index("state")
    return tree_sum_exact(jnp.where(mine, cands, 0.0), "state")


def analyse(current, observed, target, noise):
    m_loc = current.shape[0]
    n_member = lax.axis_size("member")
    count = m_loc * n_member
    me = lax.axis_index("member")
    n_rows = current.shape[1]
    obs = observed.shape[1]

    row_loc = jnp.mean(current, axis=0)
    obs_loc = jnp.mean(observed, axis=0)
    row_c = current - row_loc[None, :]
    obs_c = observed - obs_loc[None, :]
    gram_loc = tdot(obs_c, obs_c)
    cross_loc = tdot(obs_c, row_c)

    size = 128 if obs % 128 == 0 else obs
    nb = obs // size
    pairs = [(i, j) for i in range(nb) for j in range(i + 1)]
    width = -(-(obs + n_rows) // size) * size
    slots = jnp.zeros((n_member, width), jnp.float32)
    slots = lax.dynamic_update_slice(slots, jnp.concatenate([obs_loc, row_loc])[None, :], (me, 0))
    pieces = [gram_loc[i * size:(i + 1) * size, j * size:(j + 1) * size] for i, j in pairs]
    packed = jnp.concatenate(pieces + [slots.reshape(-1, size)], axis=0)
    packed = tree_sum(packed, "member")
    gram_blocks = packed[: len(pairs) * size]
    slots = packed[len(pairs) * size:].reshape(n_member, width)[:, : obs + n_rows]
    cross_sum = tree_sum(cross_loc, "member")

    means = jnp.mean(slots, axis=0)
    dev = slots - means[None, :]
    obs_mean = means[:obs]
    dev_obs = dev[:, :obs]
    dev_row = dev[:, obs:]

    corr = m_loc * tdot(dev_obs, dev_obs)
    blk = [[None] * nb for _ in range(nb)]
    for p, (i, j) in enumerate(pairs):
        part = gram_blocks[p * size:(p + 1) * size] + corr[i * size:(i + 1) * size, j * size:(j + 1) * size]
        part = part / (count - 1.0)
        if i == j:
            part = part + jnp.eye(size, dtype=part.dtype) * noise[i * size:(i + 1) * size][None, :]
        blk[i][j] = part
    obs_anom = observed - obs_mean[None, :]
    rhs = (target - obs_mean)[:, None] - 0.5 * obs_anom.T
    gain = block_solve(blk, rhs, size)

    cross = (cross_sum + m_loc * tdot(dev_obs, dev_row)) / (count - 1.0)
    return gain, cross


def shards(state, obs_values, noise_var, obs_rows, owner):
    num_blocks = obs_rows.shape[0]
    current = state
    onehot = (jnp.arange(current.shape[1], dtype=obs_rows.dtype)[:, None] == obs_rows[0][None, :]).astype(current.dtype)
    cands = full_dot(current, onehot)
    for block in range(num_blocks):
        observed = exchange(cands, owner[block])
        gain, cross = analyse(current, observed, obs_values[block], noise_var[block])
        if block + 1 < num_blocks:
            rows = obs_rows[block + 1]
            picked = jnp.take(current, rows, axis=1)
            cands = picked + full_dot(gain.T, jnp.take(cross, rows, axis=1))
        current = current + full_dot(gain.T, cross)
    return current


def solution(mesh):
    placed = (P("member", "state"), P(), P(), P(), P())
    return jax.shard_map(
        shards, mesh=mesh, in_specs=placed, out_specs=P("member", "state"), check_vma=False
    )
```

```python
import jax
import jax.numpy as jnp
from jax import lax
from jax.sharding import PartitionSpec as P


def full_dot(left, right):
    return jnp.dot(left, right, precision=lax.Precision.HIGHEST, preferred_element_type=jnp.float32)


def tdot(left, right):
    return lax.dot_general(
        left, right, (((0,), (0,)), ((), ())),
        precision=lax.Precision.HIGHEST, preferred_element_type=jnp.float32,
    )


def _pow2(n):
    return n > 0 and (n & (n - 1)) == 0


def tree_sum(x, axis):
    n = lax.axis_size(axis)
    if n == 1:
        return x
    if not _pow2(n) or x.shape[0] % n != 0:
        return lax.psum(x, axis)
    me = lax.axis_index(axis)
    cur = x
    k = 1
    while k < n:
        perm = [(i, i ^ k) for i in range(n)]
        h = cur.shape[0] // 2
        bit = (me // k) % 2
        keep = lax.dynamic_slice_in_dim(cur, bit * h, h, axis=0)
        away = lax.dynamic_slice_in_dim(cur, (1 - bit) * h, h, axis=0)
        cur = keep + lax.ppermute(away, axis, perm)
        k *= 2
    k = n // 2
    while k >= 1:
        perm = [(i, i ^ k) for i in range(n)]
        bit = (me // k) % 2
        other = lax.ppermute(cur, axis, perm)
        cur = jnp.where(bit == 0, jnp.concatenate([cur, other]), jnp.concatenate([other, cur]))
        k //= 2
    return cur


def tree_sum_exact(x, axis):
    n = lax.axis_size(axis)
    if not _pow2(n):
        return lax.psum(x, axis)
    k = 1
    while k < n:
        perm = [(i, i ^ k) for i in range(n)]
        x = x + lax.ppermute(x, axis, perm)
        k *= 2
    return x


def block_solve(blk, right, size):
    nb = len(blk)
    eye = jnp.eye(size, dtype=right.dtype)
    rhs = [right[i * size:(i + 1) * size] for i in range(nb)]
    low = [[None] * nb for _ in range(nb)]
    inv = [None] * nb
    fwd = [None] * nb
    for k in range(nb):
        diag = lax.linalg.cholesky(blk[k][k], symmetrize_input=False)
        inv[k] = lax.linalg.triangular_solve(diag, eye, left_side=True, lower=True)
        fwd[k] = full_dot(inv[k], rhs[k])
        for i in range(k + 1, nb):
            low[i][k] = full_dot(blk[i][k], inv[k].T)
        for i in range(k + 1, nb):
            for j in range(k + 1, i + 1):
                blk[i][j] = blk[i][j] - full_dot(low[i][k], low[j][k].T)
            rhs[i] = rhs[i] - full_dot(low[i][k], fwd[k])
    out = [None] * nb
    for k in reversed(range(nb)):
        acc = fwd[k]
        for j in range(k + 1, nb):
            acc = acc - tdot(low[j][k], out[j])
        out[k] = tdot(inv[k], acc)
    return jnp.concatenate(out, axis=0)


def exchange(cands, owners_block):
    obs = cands.shape[1]
    tile = obs // owners_block.shape[0]
    own_each = jnp.repeat(owners_block, tile)
    mine = own_each[None, :] == lax.axis_index("state")
    return tree_sum_exact(jnp.where(mine, cands, 0.0), "state")


def analyse(current, observed, target, noise):
    m_loc = current.shape[0]
    n_member = lax.axis_size("member")
    count = m_loc * n_member
    me = lax.axis_index("member")
    n_rows = current.shape[1]
    obs = observed.shape[1]

    row_loc = jnp.mean(current, axis=0)
    obs_loc = jnp.mean(observed, axis=0)
    row_c = current - row_loc[None, :]
    obs_c = observed - obs_loc[None, :]
    gram_loc = tdot(obs_c, obs_c)
    cross_loc = tdot(obs_c, row_c)

    size = 128 if obs % 128 == 0 else obs
    nb = obs // size
    pairs = [(i, j) for i in range(nb) for j in range(i + 1)]
    width = -(-(obs + n_rows) // size) * size
    slots = jnp.zeros((n_member, width), jnp.float32)
    slots = lax.dynamic_update_slice(slots, jnp.concatenate([obs_loc, row_loc])[None, :], (me, 0))
    pieces = [gram_loc[i * size:(i + 1) * size, j * size:(j + 1) * size] for i, j in pairs]
    packed = jnp.concatenate(pieces + [slots.reshape(-1, size)], axis=0)
    packed = tree_sum(packed, "member")
    gram_blocks = packed[: len(pairs) * size]
    slots = packed[len(pairs) * size:].reshape(n_member, width)[:, : obs + n_rows]
    cross_sum = tree_sum(cross_loc, "member")

    means = jnp.mean(slots, axis=0)
    dev = slots - means[None, :]
    obs_mean = means[:obs]
    dev_obs = dev[:, :obs]
    dev_row = dev[:, obs:]

    corr = m_loc * tdot(dev_obs, dev_obs)
    blk = [[None] * nb for _ in range(nb)]
    for p, (i, j) in enumerate(pairs):
        part = gram_blocks[p * size:(p + 1) * size] + corr[i * size:(i + 1) * size, j * size:(j + 1) * size]
        part = part / (count - 1.0)
        if i == j:
            part = part + jnp.eye(size, dtype=part.dtype) * noise[i * size:(i + 1) * size][None, :]
        blk[i][j] = part
    obs_anom = observed - obs_mean[None, :]
    rhs = (target - obs_mean)[:, None] - 0.5 * obs_anom.T
    gain = block_solve(blk, rhs, size)

    cross = (cross_sum + m_loc * tdot(dev_obs, dev_row)) / (count - 1.0)
    return gain, cross


def shards(state, obs_values, noise_var, obs_rows, owner):
    num_blocks = obs_rows.shape[0]
    current = state
    onehot = (jnp.arange(current.shape[1], dtype=obs_rows.dtype)[:, None] == obs_rows[0][None, :]).astype(current.dtype)
    cands = full_dot(current, onehot)
    for block in range(num_blocks):
        observed = exchange(cands, owner[block])
        gain, cross = analyse(current, observed, obs_values[block], noise_var[block])
        if block + 1 < num_blocks:
            rows = obs_rows[block + 1]
            pick_rows = (jnp.arange(current.shape[1], dtype=rows.dtype)[:, None] == rows[None, :]).astype(current.dtype)
            picked = full_dot(current, pick_rows)
            pick_next = (jnp.arange(cross.shape[1], dtype=rows.dtype)[:, None] == rows[None, :]).astype(cross.dtype)
            cands = picked + full_dot(gain.T, full_dot(cross, pick_next))
        current = current + full_dot(gain.T, cross)
    return current


def solution(mesh):
    placed = (P("member", "state"), P(), P(), P(), P())
    return jax.shard_map(
        shards, mesh=mesh, in_specs=placed, out_specs=P("member", "state"), check_vma=False
    )
```
